256 devices in a mesh: line: 8 (over x, core), grp: 32 (over y, z).
Axes of the slice: x: 4, y: 4, z: 8, core: 2. Of those that a mesh axis runs over, the one named last changes fastest.
Arguments:
- shot_traces: float32 [512, 192, 4096], P(('line', 'grp')), may hold values from -6 to 6
- aperture: int32 [256, 3, 32, 16], replicated, may hold values from -1 to 95, as said below
- taper_index: int32 [256, 3, 32, 16], P(('line', 'grp')), may hold values from 0 to 7
- taper_table: float32 [8, 2], replicated, may hold values from 0.2 to 1
Outputs:
- multiples: float32 [512, 192, 2, 128], P(('line', 'grp'))
The draws below stay inside these ranges and needn't reach their ends.
Inputs may be any that keep to these rules, and one draw needn't show every extreme that they name: `aperture`: each entry is -1 for an empty slot, or r = q * 32 + h with q - s between -1 and 1, s being the entry's second index.
All inputs are finite; a program needn't handle non-finite values.
Results may differ from the reference program's by a relative error of at most 0.0003.
Values sent between devices are 32-bit elements; how exact they have to be, the bound alone decides.
No kernel may reach another device: no remote copies, remote signals or barrier semaphores. Data moves between devices by JAX's collectives and lax.ppermute only.
A program may use at most 128 MiB of HBM per device.

```python
import jax
import jax.numpy as jnp
from jax import lax

NT = 4096
NF = 128
BP = 2
CAP = 16
NTAPER = 8
LINES = 8
GROUPS = 32
KDEV = 256
SHOTS = 512
RECV = 192


def draw_aperture(key, part):
    key_side, key_group, key_live, key_rate = jax.random.split(key, 4)
    layout = (LINES * GROUPS, 3, GROUPS, CAP)
    side_row = lax.broadcasted_iota(jnp.int32, layout, 1)
    offset = jax.random.randint(key_side, layout, -1, 2)
    target_line = jnp.clip(side_row + offset, 0, 2)
    target_group = jax.random.randint(key_group, layout, 0, GROUPS)
    live_rate = jax.random.randint(key_rate, (LINES * GROUPS, 1, 1, 1), 4, 10)
    is_live = jax.random.randint(key_live, layout, 0, 10) < live_rate
    blocks = jnp.where(is_live, target_line * GROUPS + target_group, -1)
    blocks = blocks.at[0, 1, 0, 0].set(3 * GROUPS - 1)
    blocks = blocks.at[0, 1, 0, 1].set(-1)
    return blocks.astype(jnp.int32)


def with_ends(array, key, least, top_value):
    shape = array.shape
    spot = [jax.random.randint(jax.random.fold_in(key, axis), (), 0, shape[axis]) for axis in range(len(shape))]
    array = array.at[tuple(spot)].set(least)
    longest = shape.index(max(shape))
    spot[longest] = (spot[longest] + 1) % shape[longest]
    return array.at[tuple(spot)].set(top_value)


def levels(own_key, shape, cuts, least, largest):
    factor_of = 1.0
    for dim, blocks in cuts:
        draws = jax.random.uniform(jax.random.fold_in(jax.random.fold_in(own_key, 6), dim), (blocks,), jnp.float32, least / len(cuts), largest / len(cuts))
        factor_of = factor_of * jnp.repeat(jnp.exp(draws), shape[dim] // blocks).reshape((-1,) + (1,) * (len(shape) - 1 - dim))
    return factor_of


def normal_values(key, shape, deviation, bound, shards=(), held_as=jnp.bfloat16):
    values = jax.random.normal(key, shape, jnp.float32) * deviation
    if len(shards) > 0:
        values = levels(key, shape, shards, -0.22, 0.18) * values
    return jnp.clip(values, min=-bound, max=bound).astype(held_as)


def setup_inputs(seed: int = 0) -> dict:
    splits = jax.random.split(jax.random.key(seed), 5)
    return {
        "shot_traces": normal_values(splits[0], (SHOTS, RECV, NT), 1.0, 6.0, ((0, 256),), jnp.float32),
        "aperture": draw_aperture(jax.random.fold_in(splits[4], 71), 0),
        "taper_index": with_ends(jax.random.randint(splits[2], (KDEV, 3, GROUPS, CAP), 0, NTAPER), jax.random.fold_in(splits[2], 1), 0, NTAPER - 1).astype(jnp.int32),
        "taper_table": jnp.clip(jax.random.uniform(splits[3], (NTAPER, BP), jnp.float32, 0.2, 1.0), 0.2, 1.0),
    }


def spectra_of(shot_traces):
    def one_shot(traces):
        spectrum_rows = jnp.fft.rfft(traces, axis=-1, norm="ortho")[:, :NF]
        return jnp.stack([jnp.real(spectrum_rows), jnp.imag(spectrum_rows)], axis=1)
    return lax.map(one_shot, shot_traces)


def combine(column, picked, weight):
    col_real = column[:, :, None, :, :, None, 0, :]
    col_imag = column[:, :, None, :, :, None, 1, :]
    scaled = picked * weight[:, :, :, :, None, None, None]
    row_real = scaled[:, :, :, None, :, :, 0, :]
    row_imag = scaled[:, :, :, None, :, :, 1, :]
    prod_real = -jnp.sum(col_real * row_real - col_imag * row_imag, axis=4)
    prod_imag = -jnp.sum(col_real * row_imag + col_imag * row_real, axis=4)
    return jnp.stack([prod_real, prod_imag], axis=5)


def reference(shot_traces, aperture, taper_index, taper_table):
    spectra = spectra_of(shot_traces)
    blocks = spectra.reshape(LINES, GROUPS, BP, 3, GROUPS, BP, 2, NF)
    list_table = aperture.reshape(LINES, GROUPS, 3, GROUPS, CAP)
    pick_table = taper_index.reshape(LINES, GROUPS, 3, GROUPS, CAP)
    side_index = jnp.arange(3, dtype=jnp.int32)
    group_range = jnp.arange(GROUPS, dtype=jnp.int32)
    running = jnp.zeros((LINES, GROUPS, BP, 3, GROUPS, BP, 2, NF), blocks.dtype)

    def visit_block(running, surface):
        line_pos = (surface // GROUPS).astype(jnp.int32)
        group_pos = (surface % GROUPS).astype(jnp.int32)
        anchor = jnp.zeros((), jnp.int32)
        row_tile = lax.dynamic_slice(blocks, (line_pos, group_pos, anchor, anchor, anchor, anchor, anchor, anchor), (1, 1, BP, 3, GROUPS, BP, 2, NF))
        row_tile = row_tile.reshape(BP, 3 * GROUPS, BP, 2, NF)
        columns = []
        for side_line in range(3):
            shot_line = ((line_pos + side_line - 1 + LINES) % LINES).astype(jnp.int32)
            column_tile = lax.dynamic_slice(blocks, (shot_line, anchor, anchor, jnp.asarray(2 - side_line, jnp.int32), group_pos, anchor, anchor, anchor), (1, GROUPS, BP, 1, 1, BP, 2, NF))
            columns.append(column_tile.reshape(GROUPS, BP, BP, 2, NF))
        column = jnp.stack(columns)
        slot_list = lax.dynamic_index_in_dim(lax.dynamic_index_in_dim(list_table, line_pos, 0, False), group_pos, 0, False)
        chosen = lax.dynamic_index_in_dim(lax.dynamic_index_in_dim(pick_table, line_pos, 0, False), group_pos, 0, False)
        is_live = slot_list >= 0
        safe_rows = jnp.maximum(slot_list, 0).astype(jnp.int32)
        picked = jnp.take(row_tile, safe_rows.reshape(-1), axis=1).reshape(BP, 3, GROUPS, CAP, BP, 2, NF)
        picked = jnp.transpose(picked, (1, 2, 3, 0, 4, 5, 6))
        weight = taper_table[chosen] * is_live[..., None].astype(taper_table.dtype)
        partial_value = combine(column, picked, weight)
        recv_line = safe_rows // GROUPS
        recv_group = safe_rows % GROUPS
        out_line = jnp.clip(recv_line - side_index[:, None, None] + 1, 0, 2).astype(jnp.int32)
        shot_lines = ((line_pos + side_index - 1 + LINES) % LINES).astype(jnp.int32)
        running = running.at[shot_lines[:, None, None], group_range[None, :, None], :, out_line, recv_group].add(partial_value)
        return running, None

    running, _ = lax.scan(visit_block, running, jnp.arange(KDEV, dtype=jnp.int32))
    return running.reshape(SHOTS, RECV, 2, NF)
```

```python
import math

import jax
import jax.numpy as jnp
from jax import lax
from jax.sharding import PartitionSpec as P

NF = 128
BP = 2
CAP = 16
RADIX = 64

HIGHEST = lax.Precision.HIGHEST


def dft_matrix(samples):
    inner = samples // RADIX
    major = jnp.arange(RADIX, dtype=jnp.int32)
    minor = jnp.arange(inner, dtype=jnp.int32)
    bins = jnp.arange(NF, dtype=jnp.int32)
    step = 2.0 * math.pi / samples
    angle_a = ((major[:, None] * inner * bins[None, :]) % samples).astype(jnp.float32) * step
    angle_n = ((minor[:, None] * bins[None, :]) % samples).astype(jnp.float32) * step
    a_re, a_im = jnp.cos(angle_a), -jnp.sin(angle_a)
    n_re, n_im = jnp.cos(angle_n), -jnp.sin(angle_n)
    scale = 1.0 / math.sqrt(samples)
    c_re = (a_re[:, None, :] * n_re[None, :, :] - a_im[:, None, :] * n_im[None, :, :]) * scale
    c_im = (a_re[:, None, :] * n_im[None, :, :] + a_im[:, None, :] * n_re[None, :, :]) * scale
    return jnp.concatenate([c_re, c_im], axis=-1).reshape(samples, 2 * NF)


def spectrum(traces, table):
    shots, recv, samples = traces.shape
    out = jnp.dot(traces.reshape(shots * recv, samples), table, precision=HIGHEST)
    return out.reshape(shots, recv // BP, BP, 2, NF)


def combine(side_cols, weight, gathered):
    scaled = gathered * jnp.transpose(weight, (0, 2, 1))[:, :, :, None, None, None]
    col_re = side_cols[:, :, :, None, None, 0, :]
    col_im = side_cols[:, :, :, None, None, 1, :]
    row_re = scaled[None, :, :, :, :, 0, :]
    row_im = scaled[None, :, :, :, :, 1, :]
    prod_re = -jnp.sum(col_re * row_re - col_im * row_im, axis=(1, 2))
    prod_im = -jnp.sum(col_re * row_im + col_im * row_re, axis=(1, 2))
    return jnp.stack([prod_re, prod_im], axis=3)


def body(shot_traces, aperture, taper_index, taper_table):
    group_count = lax.axis_size("grp")
    line_count = lax.axis_size("line")
    my_line = lax.axis_index("line")
    my_group = lax.axis_index("grp")
    shots, recv, samples = shot_traces.shape
    sides = 3
    width = recv // (BP * sides)
    blocks = sides * width
    up = [(i, (i + 1) % line_count) for i in range(line_count)]
    down = [((i + 1) % line_count, i) for i in range(line_count)]

    tapers = lax.all_gather(taper_index.reshape(sides, group_count, CAP), "grp", axis=0, tiled=False)
    tapers = lax.dynamic_index_in_dim(tapers, my_group, 2, False)
    full_table = aperture.reshape(line_count, group_count, sides, group_count, CAP)
    slot_list = lax.dynamic_index_in_dim(
        lax.dynamic_index_in_dim(full_table, my_line, 0, False), my_group, 2, False
    )
    taper_rows = taper_table.shape[0]
    pick = tapers[..., None] == jnp.arange(taper_rows, dtype=jnp.int32)
    slot_weight = jnp.sum(
        jnp.where(pick[..., None], taper_table[None, None, None, :, :], 0.0), axis=3
    )
    hit = slot_list[..., None] == jnp.arange(blocks, dtype=jnp.int32)
    weight = jnp.sum(
        jnp.where(hit[..., None], slot_weight[:, :, :, None, :], 0.0), axis=2
    )

    table = dft_matrix(samples)
    thirds = [
        spectrum(lax.slice_in_dim(shot_traces, q * width * BP, (q + 1) * width * BP, axis=1), table)
        for q in range(sides)
    ]
    side_cols = [
        lax.ppermute(thirds[2], "line", up),
        thirds[1],
        lax.ppermute(thirds[0], "line", down),
    ]
    gathered = [lax.all_gather(t, "grp", axis=0, tiled=False) for t in thirds]

    parts = {}
    for q in range(sides):
        for s in range(sides):
            if not 0 <= q + 1 - s < sides:
                continue
            w = weight[:, s, q * width:(q + 1) * width, :]
            parts[s, q] = combine(side_cols[s], w, gathered[q])

    to_down = jnp.concatenate([parts[0, 0], parts[0, 1]], axis=1)
    to_up = jnp.concatenate([parts[2, 1], parts[2, 2]], axis=1)
    from_up = lax.ppermute(to_down, "line", down)
    from_down = lax.ppermute(to_up, "line", up)
    local = jnp.concatenate([parts[1, q] for q in range(sides)], axis=1)
    result = local
    result = result.at[:, width:].add(from_up)
    result = result.at[:, : 2 * width].add(from_down)
    return result.reshape(shots, recv, 2, NF)


def solution(mesh):
    return jax.shard_map(
        body,
        mesh=mesh,
        in_specs=(P(("line", "grp"), None, None), P(), P(("line", "grp"), None, None, None), P()),
        out_specs=P(("line", "grp"), None, None, None),
        check_vma=False,
    )
```

```python
import math

import jax
import jax.numpy as jnp
import numpy as np
from jax import lax
from jax.sharding import Mesh, NamedSharding
from jax.sharding import PartitionSpec as P

NF = 128
BP = 2
CAP = 16
RADIX = 64

HIGHEST = lax.Precision.HIGHEST


def dft_matrix(samples):
    inner = samples // RADIX
    major = jnp.arange(RADIX, dtype=jnp.int32)
    minor = jnp.arange(inner, dtype=jnp.int32)
    bins = jnp.arange(NF, dtype=jnp.int32)
    step = 2.0 * math.pi / samples
    angle_a = ((major[:, None] * inner * bins[None, :]) % samples).astype(jnp.float32) * step
    angle_n = ((minor[:, None] * bins[None, :]) % samples).astype(jnp.float32) * step
    a_re, a_im = jnp.cos(angle_a), -jnp.sin(angle_a)
    n_re, n_im = jnp.cos(angle_n), -jnp.sin(angle_n)
    scale = 1.0 / math.sqrt(samples)
    c_re = (a_re[:, None, :] * n_re[None, :, :] - a_im[:, None, :] * n_im[None, :, :]) * scale
    c_im = (a_re[:, None, :] * n_im[None, :, :] + a_im[:, None, :] * n_re[None, :, :]) * scale
    return jnp.concatenate([c_re, c_im], axis=-1).reshape(samples, 2 * NF)


def spectrum(traces, table):
    shots, recv, samples = traces.shape
    out = jnp.dot(traces.reshape(shots * recv, samples), table, precision=HIGHEST)
    return out.reshape(shots, recv // BP, BP, 2, NF)


def combine(side_cols, weight, gathered):
    scaled = gathered[None] * jnp.transpose(weight, (0, 1, 3, 2))[:, :, :, :, None, None, None]
    col_re = side_cols[:, :, :, :, None, None, 0, :]
    col_im = side_cols[:, :, :, :, None, None, 1, :]
    row_re = scaled[:, None, :, :, :, :, 0, :]
    row_im = scaled[:, None, :, :, :, :, 1, :]
    prod_re = -jnp.sum(col_re * row_re - col_im * row_im, axis=(2, 3))
    prod_im = -jnp.sum(col_re * row_im + col_im * row_re, axis=(2, 3))
    return jnp.stack([prod_re, prod_im], axis=4)


def body(shot_traces, aperture, taper_index, taper_table):
    line_count = lax.axis_size("line")
    rows = lax.axis_size("gy")
    cols = lax.axis_size("gz")
    group_count = rows * cols
    my_line = lax.axis_index("line")
    my_row = lax.axis_index("gy")
    my_col = lax.axis_index("gz")
    shots, recv, samples = shot_traces.shape
    sides = 3
    width = recv // (BP * sides)
    up = [(i, (i + 1) % line_count) for i in range(line_count)]
    down = [((i + 1) % line_count, i) for i in range(line_count)]

    taper_rows = taper_table.shape[0]
    pick = taper_index.reshape(sides, rows, cols, CAP)[..., None] == jnp.arange(taper_rows, dtype=jnp.int32)
    src_weight = jnp.sum(jnp.where(pick[..., None], taper_table, 0.0), axis=-2)
    src_weight = lax.dynamic_index_in_dim(
        lax.all_gather(src_weight, "gz", axis=0, tiled=False), my_col, 3, False
    )
    full_table = aperture.reshape(line_count, rows, cols, sides, rows, cols, CAP)
    slot_list = lax.dynamic_index_in_dim(
        lax.dynamic_index_in_dim(
            lax.dynamic_index_in_dim(full_table, my_line, 0, False), my_row, 0, False
        ),
        my_col,
        3,
        False,
    )
    hit = slot_list[..., None] == jnp.arange(sides * width, dtype=jnp.int32)
    weight = jnp.sum(jnp.where(hit[..., None], src_weight[:, :, :, :, None, :], 0.0), axis=3)
    weight = jnp.transpose(weight, (1, 2, 0, 3, 4))

    table = dft_matrix(samples)
    thirds = [
        spectrum(lax.slice_in_dim(shot_traces, q * width * BP, (q + 1) * width * BP, axis=1), table)
        for q in range(sides)
    ]
    gathered = [lax.all_gather(t, "gz", axis=0, tiled=False) for t in thirds]

    stacked = jnp.stack(thirds).reshape(sides, shots, rows, cols, BP, 2, NF)
    spread = lax.all_to_all(stacked, "gy", split_axis=2, concat_axis=2, tiled=True)
    spread = jnp.transpose(spread, (0, 2, 1, 3, 4, 5, 6))
    side_cols = [
        lax.ppermute(spread[2], "line", up),
        spread[1],
        lax.ppermute(spread[0], "line", down),
    ]

    parts = {}
    for q in range(sides):
        for s in range(sides):
            if not 0 <= q + 1 - s < sides:
                continue
            w = weight[s, :, :, q * width:(q + 1) * width, :]
            local = combine(side_cols[s], w, gathered[q])
            parts[s, q] = lax.psum_scatter(local, "gy", scatter_dimension=0, tiled=False)

    to_down = jnp.concatenate([parts[0, 0], parts[0, 1]], axis=1)
    to_up = jnp.concatenate([parts[2, 1], parts[2, 2]], axis=1)
    from_up = lax.ppermute(to_down, "line", down)
    from_down = lax.ppermute(to_up, "line", up)
    result = jnp.concatenate([parts[1, q] for q in range(sides)], axis=1)
    result = result.at[:, width:].add(from_up)
    result = result.at[:, : 2 * width].add(from_down)
    return result.reshape(shots, recv, 2, NF)


def grid_shape(mesh):
    row = mesh.devices[0]
    try:
        ys = sorted({d.coords[1] for d in row})
        zs = sorted({d.coords[2] for d in row})
        if len(ys) * len(zs) == len(row):
            return len(ys), len(zs)
    except Exception:
        pass
    return 4, len(row) // 4


def solution(mesh):
    rows, cols = grid_shape(mesh)
    lines = mesh.devices.shape[0]
    fine = Mesh(np.asarray(mesh.devices).reshape(lines, rows, cols), ("line", "gy", "gz"))
    split = ("line", "gy", "gz")
    mapped = jax.shard_map(
        body,
        mesh=fine,
        in_specs=(P(split, None, None), P(), P(split, None, None, None), P()),
        out_specs=P(split, None, None, None),
        check_vma=False,
    )
    out_sharding = NamedSharding(mesh, P(("line", "grp"), None, None, None))
    return jax.jit(mapped, out_shardings=out_sharding)
```

```python
import math

import jax
import jax.numpy as jnp
import numpy as np
from jax import lax
from jax.sharding import Mesh, NamedSharding
from jax.sharding import PartitionSpec as P

NF = 128
BP = 2
CAP = 16
RADIX = 64

HIGH = lax.Precision.HIGH


def dft_matrix(samples):
    inner = samples // RADIX
    major = jnp.arange(RADIX, dtype=jnp.int32)
    minor = jnp.arange(inner, dtype=jnp.int32)
    bins = jnp.arange(NF, dtype=jnp.int32)
    step = 2.0 * math.pi / samples
    angle_a = ((major[:, None] * inner * bins[None, :]) % samples).astype(jnp.float32) * step
    angle_n = ((minor[:, None] * bins[None, :]) % samples).astype(jnp.float32) * step
    a_re, a_im = jnp.cos(angle_a), -jnp.sin(angle_a)
    n_re, n_im = jnp.cos(angle_n), -jnp.sin(angle_n)
    scale = 1.0 / math.sqrt(samples)
    c_re = (a_re[:, None, :] * n_re[None, :, :] - a_im[:, None, :] * n_im[None, :, :]) * scale
    c_im = (a_re[:, None, :] * n_im[None, :, :] + a_im[:, None, :] * n_re[None, :, :]) * scale
    return jnp.concatenate([c_re, c_im], axis=-1).reshape(samples, 2 * NF)


def spectrum(traces, table):
    shots, recv, samples = traces.shape
    out = jnp.dot(traces.reshape(shots * recv, samples), table, precision=HIGH)
    return out.reshape(shots, recv // BP, BP, 2, NF)


def combine(side_cols, weight, block):
    scaled = block[None] * jnp.transpose(weight, (0, 2, 1))[:, :, :, None, None, None]
    col_re = side_cols[:, :, :, None, None, 0, :]
    col_im = side_cols[:, :, :, None, None, 1, :]
    row_re = scaled[:, None, :, :, :, 0, :]
    row_im = scaled[:, None, :, :, :, 1, :]
    prod_re = -jnp.sum(col_re * row_re - col_im * row_im, axis=2)
    prod_im = -jnp.sum(col_re * row_im + col_im * row_re, axis=2)
    return jnp.stack([prod_re, prod_im], axis=4)


def body(shot_traces, aperture, taper_index, taper_table):
    line_count = lax.axis_size("line")
    rows = lax.axis_size("gy")
    cols = lax.axis_size("gz")
    my_line = lax.axis_index("line")
    my_row = lax.axis_index("gy")
    my_col = lax.axis_index("gz")
    shots, recv, samples = shot_traces.shape
    sides = 3
    width = recv // (BP * sides)
    blocks = sides * width
    up = [(i, (i + 1) % line_count) for i in range(line_count)]
    down = [((i + 1) % line_count, i) for i in range(line_count)]
    right = [(i, (i + 1) % cols) for i in range(cols)]
    left = [((i + 1) % cols, i) for i in range(cols)]
    spans = [(0, 2 * width), (0, blocks), (width, blocks)]

    taper_rows = taper_table.shape[0]
    pick = taper_index.reshape(sides, rows, cols, CAP)[..., None] == jnp.arange(taper_rows, dtype=jnp.int32)
    src_weight = jnp.sum(jnp.where(pick[..., None], taper_table, 0.0), axis=-2)
    full_table = aperture.reshape(line_count, rows, cols, sides, rows, cols, CAP)
    slot_table = lax.dynamic_index_in_dim(
        lax.dynamic_index_in_dim(
            lax.dynamic_index_in_dim(full_table, my_line, 0, False), my_row, 0, False
        ),
        my_col,
        3,
        False,
    )

    table = dft_matrix(samples)
    own = spectrum(shot_traces, table)

    stacked = own.reshape(shots, sides, rows, cols, BP, 2, NF)
    stacked = jnp.transpose(stacked, (1, 0, 2, 3, 4, 5, 6))
    spread = lax.all_to_all(stacked, "gy", split_axis=2, concat_axis=2, tiled=True)
    spread = jnp.transpose(spread, (0, 2, 1, 3, 4, 5, 6))
    side_cols = [
        lax.ppermute(spread[2], "line", up),
        spread[1],
        lax.ppermute(spread[0], "line", down),
    ]

    spec_size = own.size
    payload = jnp.concatenate([own.reshape(-1), src_weight.reshape(-1)])

    def contribution(carried, source):
        block = carried[:spec_size].reshape(own.shape)
        weights = lax.dynamic_index_in_dim(
            carried[spec_size:].reshape(src_weight.shape), my_col, 2, False
        )
        slots = lax.dynamic_index_in_dim(slot_table, source, 0, False)
        hit = slots[..., None] == jnp.arange(blocks, dtype=jnp.int32)
        dense = jnp.sum(jnp.where(hit[..., None], weights[:, :, :, None, :], 0.0), axis=2)
        out = []
        for s in range(sides):
            lo, hi = spans[s]
            cols_s = lax.dynamic_index_in_dim(side_cols[s], source, 2, False)
            out.append(combine(cols_s, dense[s, :, lo:hi], block[:, lo:hi]))
        return out

    def accumulate(total, extra):
        return [t + e for t, e in zip(total, extra)]

    total = contribution(payload, my_col)
    forward = payload
    backward = payload
    for step in range(1, cols // 2 + 1):
        forward = lax.ppermute(forward, "gz", right)
        total = accumulate(total, contribution(forward, (my_col - step) % cols))
        if 2 * step < cols:
            backward = lax.ppermute(backward, "gz", left)
            total = accumulate(total, contribution(backward, (my_col + step) % cols))

    merged = jnp.concatenate(total, axis=2)
    mine = lax.psum_scatter(merged, "gy", scatter_dimension=0, tiled=False)
    first, middle = 2 * width, 2 * width + blocks
    from_up = lax.ppermute(mine[:, :first], "line", down)
    from_down = lax.ppermute(mine[:, middle:], "line", up)
    result = mine[:, first:middle]
    result = result.at[:, width:].add(from_up)
    result = result.at[:, : 2 * width].add(from_down)
    return result.reshape(shots, recv, 2, NF)


def grid_shape(mesh):
    row = mesh.devices[0]
    try:
        ys = sorted({d.coords[1] for d in row})
        zs = sorted({d.coords[2] for d in row})
        if len(ys) * len(zs) == len(row):
            return len(ys), len(zs)
    except Exception:
        pass
    return 4, len(row) // 4


def solution(mesh):
    rows, cols = grid_shape(mesh)
    lines = mesh.devices.shape[0]
    fine = Mesh(np.asarray(mesh.devices).reshape(lines, rows, cols), ("line", "gy", "gz"))
    split = ("line", "gy", "gz")
    mapped = jax.shard_map(
        body,
        mesh=fine,
        in_specs=(P(split, None, None), P(), P(split, None, None, None), P()),
        out_specs=P(split, None, None, None),
        check_vma=False,
    )
    out_sharding = NamedSharding(mesh, P(("line", "grp"), None, None, None))
    return jax.jit(mapped, out_shardings=out_sharding)
```

```python
import math

import jax
import jax.numpy as jnp
import numpy as np
from jax import lax
from jax.sharding import Mesh, NamedSharding
from jax.sharding import PartitionSpec as P

NF = 128
BP = 2
CAP = 16
RADIX = 64

HIGH = lax.Precision.HIGH


def dft_matrix(samples):
    inner = samples // RADIX
    major = jnp.arange(RADIX, dtype=jnp.int32)
    minor = jnp.arange(inner, dtype=jnp.int32)
    bins = jnp.arange(NF, dtype=jnp.int32)
    step = 2.0 * math.pi / samples
    angle_a = ((major[:, None] * inner * bins[None, :]) % samples).astype(jnp.float32) * step
    angle_n = ((minor[:, None] * bins[None, :]) % samples).astype(jnp.float32) * step
    a_re, a_im = jnp.cos(angle_a), -jnp.sin(angle_a)
    n_re, n_im = jnp.cos(angle_n), -jnp.sin(angle_n)
    scale = 1.0 / math.sqrt(samples)
    c_re = (a_re[:, None, :] * n_re[None, :, :] - a_im[:, None, :] * n_im[None, :, :]) * scale
    c_im = (a_re[:, None, :] * n_im[None, :, :] + a_im[:, None, :] * n_re[None, :, :]) * scale
    return jnp.concatenate([c_re, c_im], axis=-1).reshape(samples, 2 * NF)


def spectrum(traces, table):
    shots, recv, samples = traces.shape
    out = jnp.dot(traces.reshape(shots * recv, samples), table, precision=HIGH)
    return out.reshape(shots, recv // BP, BP, 2, NF)


def combine(cols, weight, block):
    scaled = block[None] * weight[:, :, :, None, None, :, None]
    col_re = cols[:, :, :, :, None, 0, None, :]
    col_im = cols[:, :, :, :, None, 1, None, :]
    row_re = scaled[:, None, :, :, :, 0]
    row_im = scaled[:, None, :, :, :, 1]
    prod_re = -jnp.sum(col_re * row_re - col_im * row_im, axis=(2, 3))
    prod_im = -jnp.sum(col_re * row_im + col_im * row_re, axis=(2, 3))
    return jnp.stack([prod_re, prod_im], axis=3)


def body(shot_traces, aperture, taper_index, taper_table):
    line_count = lax.axis_size("line")
    rows = lax.axis_size("gy")
    cols = lax.axis_size("gz")
    my_line = lax.axis_index("line")
    my_row = lax.axis_index("gy")
    my_col = lax.axis_index("gz")
    shots, recv, samples = shot_traces.shape
    sides = 3
    width = recv // (BP * sides)
    blocks = sides * width
    up = [(i, (i + 1) % line_count) for i in range(line_count)]
    down = [((i + 1) % line_count, i) for i in range(line_count)]
    right = [(i, (i + 1) % cols) for i in range(cols)]
    left = [((i + 1) % cols, i) for i in range(cols)]
    spans = [(0, 2 * width), (0, blocks), (width, blocks)]

    taper_rows = taper_table.shape[0]
    pick = taper_index.reshape(sides, rows, cols, CAP)[..., None] == jnp.arange(taper_rows, dtype=jnp.int32)
    src_weight = jnp.sum(jnp.where(pick[..., None], taper_table, 0.0), axis=-2)
    full_table = aperture.reshape(line_count, rows, cols, sides, rows, cols, CAP)
    slot_table = lax.dynamic_index_in_dim(
        lax.dynamic_index_in_dim(
            lax.dynamic_index_in_dim(full_table, my_line, 0, False), my_row, 0, False
        ),
        my_col,
        3,
        False,
    )

    table = dft_matrix(samples)
    own = spectrum(shot_traces, table)

    stacked = own.reshape(shots, sides, rows, cols, BP, 2, NF)
    stacked = jnp.transpose(stacked, (1, 0, 2, 3, 4, 5, 6))
    spread = lax.all_to_all(stacked, "gy", split_axis=2, concat_axis=2, tiled=True)
    spread = jnp.transpose(spread, (0, 2, 1, 3, 4, 5, 6))
    side_cols = [
        lax.ppermute(spread[2], "line", up),
        spread[1],
        lax.ppermute(spread[0], "line", down),
    ]

    lanes = jnp.transpose(own, (0, 2, 3, 1, 4))
    spec_size = lanes.size
    payload = jnp.concatenate([lanes.reshape(-1), src_weight.reshape(-1)])
    carried = [payload]
    offsets = [0]
    forward = payload
    backward = payload
    for step in range(1, cols // 2 + 1):
        forward = lax.ppermute(forward, "gz", right)
        carried.append(forward)
        offsets.append(-step)
        if 2 * step < cols:
            backward = lax.ppermute(backward, "gz", left)
            carried.append(backward)
            offsets.append(step)
    sources = (my_col + jnp.asarray(offsets, dtype=jnp.int32)) % cols
    ring = jnp.stack(carried)
    gathered = ring[:, :spec_size].reshape((len(carried),) + lanes.shape)
    weights = lax.dynamic_index_in_dim(
        ring[:, spec_size:].reshape((len(carried),) + src_weight.shape), my_col, 3, False
    )
    slots = jnp.take(slot_table, sources, axis=0)
    hit = slots[..., None] == jnp.arange(blocks, dtype=jnp.int32)
    dense = jnp.sum(jnp.where(hit[..., None], weights[:, :, :, :, None, :], 0.0), axis=3)
    dense = jnp.transpose(dense, (1, 2, 0, 4, 3))

    total = []
    for s in range(sides):
        lo, hi = spans[s]
        cols_s = jnp.take(side_cols[s], sources, axis=2)
        total.append(combine(cols_s, dense[s, :, :, :, lo:hi], gathered[:, :, :, :, lo:hi]))
    merged = jnp.concatenate(total, axis=4)
    mine = lax.psum_scatter(merged, "gy", scatter_dimension=0, tiled=False)
    first, middle = 2 * width, 2 * width + blocks
    from_up = lax.ppermute(mine[:, :, :, :first], "line", down)
    from_down = lax.ppermute(mine[:, :, :, middle:], "line", up)
    result = mine[:, :, :, first:middle]
    result = result.at[:, :, :, width:].add(from_up)
    result = result.at[:, :, :, : 2 * width].add(from_down)
    result = jnp.transpose(result, (0, 3, 1, 2, 4))
    return result.reshape(shots, recv, 2, NF)


def grid_shape(mesh):
    row = mesh.devices[0]
    try:
        ys = sorted({d.coords[1] for d in row})
        zs = sorted({d.coords[2] for d in row})
        if len(ys) * len(zs) == len(row):
            return len(ys), len(zs)
    except Exception:
        pass
    return 4, len(row) // 4


def solution(mesh):
    rows, cols = grid_shape(mesh)
    lines = mesh.devices.shape[0]
    fine = Mesh(np.asarray(mesh.devices).reshape(lines, rows, cols), ("line", "gy", "gz"))
    split = ("line", "gy", "gz")
    mapped = jax.shard_map(
        body,
        mesh=fine,
        in_specs=(P(split, None, None), P(), P(split, None, None, None), P()),
        out_specs=P(split, None, None, None),
        check_vma=False,
    )
    out_sharding = NamedSharding(mesh, P(("line", "grp"), None, None, None))
    return jax.jit(mapped, out_shardings=out_sharding)
```

```python
import math

import jax
import jax.numpy as jnp
import numpy as np
from jax import lax
from jax.sharding import Mesh, NamedSharding
from jax.sharding import PartitionSpec as P

NF = 128
BP = 2
CAP = 16
RADIX = 64

HIGH = lax.Precision.HIGH


def dft_matrix(samples):
    inner = samples // RADIX
    major = jnp.arange(RADIX, dtype=jnp.int32)
    minor = jnp.arange(inner, dtype=jnp.int32)
    bins = jnp.arange(NF, dtype=jnp.int32)
    step = 2.0 * math.pi / samples
    angle_a = ((major[:, None] * inner * bins[None, :]) % samples).astype(jnp.float32) * step
    angle_n = ((minor[:, None] * bins[None, :]) % samples).astype(jnp.float32) * step
    a_re, a_im = jnp.cos(angle_a), -jnp.sin(angle_a)
    n_re, n_im = jnp.cos(angle_n), -jnp.sin(angle_n)
    scale = 1.0 / math.sqrt(samples)
    c_re = (a_re[:, None, :] * n_re[None, :, :] - a_im[:, None, :] * n_im[None, :, :]) * scale
    c_im = (a_re[:, None, :] * n_im[None, :, :] + a_im[:, None, :] * n_re[None, :, :]) * scale
    return jnp.concatenate([c_re, c_im], axis=-1).reshape(samples, 2 * NF)


def spectrum(traces, table):
    shots, recv, samples = traces.shape
    out = jnp.dot(traces.reshape(shots * recv, samples), table, precision=HIGH)
    return out.reshape(shots, recv // BP, BP, 2, NF)


def combine(cols, weight, block):
    w = weight[:, None, :, :, None, :, None]
    col_re = cols[:, :, :, :, None, 0, None, :]
    col_im = cols[:, :, :, :, None, 1, None, :]
    row_re = block[None, None, :, :, :, 0]
    row_im = block[None, None, :, :, :, 1]
    prod_re = -jnp.sum(w * (col_re * row_re - col_im * row_im), axis=(2, 3))
    prod_im = -jnp.sum(w * (col_re * row_im + col_im * row_re), axis=(2, 3))
    return jnp.stack([prod_re, prod_im], axis=3)


def body(shot_traces, aperture, taper_index, taper_table):
    line_count = lax.axis_size("line")
    rows = lax.axis_size("gy")
    cols = lax.axis_size("gz")
    my_line = lax.axis_index("line")
    my_row = lax.axis_index("gy")
    my_col = lax.axis_index("gz")
    shots, recv, samples = shot_traces.shape
    sides = 3
    width = recv // (BP * sides)
    blocks = sides * width
    up = [(i, (i + 1) % line_count) for i in range(line_count)]
    down = [((i + 1) % line_count, i) for i in range(line_count)]
    right = [(i, (i + 1) % cols) for i in range(cols)]
    left = [((i + 1) % cols, i) for i in range(cols)]
    spans = [(0, 2 * width), (0, blocks), (width, blocks)]

    taper_rows = taper_table.shape[0]
    pick = taper_index.reshape(sides, rows, cols, CAP)[..., None] == jnp.arange(taper_rows, dtype=jnp.int32)
    src_weight = jnp.sum(jnp.where(pick[..., None], taper_table, 0.0), axis=-2)
    own_blocks = lax.dynamic_slice_in_dim(aperture, (my_line * rows + my_row) * cols, cols, axis=0)
    slot_table = lax.dynamic_index_in_dim(
        own_blocks.reshape(cols, sides, rows, cols, CAP), my_col, 3, False
    )

    table = dft_matrix(samples)
    own = spectrum(shot_traces, table)

    stacked = own.reshape(shots, sides, rows, cols, BP, 2, NF)
    stacked = jnp.transpose(stacked, (1, 0, 2, 3, 4, 5, 6))
    spread = lax.all_to_all(stacked, "gy", split_axis=2, concat_axis=2, tiled=True)
    spread = jnp.transpose(spread, (0, 2, 1, 3, 4, 5, 6))
    side_cols = [
        lax.ppermute(spread[2], "line", up),
        spread[1],
        lax.ppermute(spread[0], "line", down),
    ]

    lanes = jnp.transpose(own, (0, 2, 3, 1, 4))
    spec_size = lanes.size
    payload = jnp.concatenate([lanes.reshape(-1), src_weight.reshape(-1)])
    carried = [payload]
    offsets = [0]
    forward = payload
    backward = payload
    for step in range(1, cols // 2 + 1):
        forward = lax.ppermute(forward, "gz", right)
        carried.append(forward)
        offsets.append(-step)
        if 2 * step < cols:
            backward = lax.ppermute(backward, "gz", left)
            carried.append(backward)
            offsets.append(step)
    sources = (my_col + jnp.asarray(offsets, dtype=jnp.int32)) % cols
    ring = jnp.stack(carried)
    gathered = ring[:, :spec_size].reshape((len(carried),) + lanes.shape)
    weights = lax.dynamic_index_in_dim(
        ring[:, spec_size:].reshape((len(carried),) + src_weight.shape), my_col, 3, False
    )
    slots = jnp.take(slot_table, sources, axis=0)
    hit = slots[..., None] == jnp.arange(blocks, dtype=jnp.int32)
    dense = jnp.sum(jnp.where(hit[..., None], weights[:, :, :, :, None, :], 0.0), axis=3)
    dense = jnp.transpose(dense, (1, 2, 0, 4, 3))

    def side_part(s):
        lo, hi = spans[s]
        cols_s = jnp.take(side_cols[s], sources, axis=2)
        return combine(cols_s, dense[s, :, :, :, lo:hi], gathered[:, :, :, :, lo:hi])

    outer = jnp.concatenate([side_part(0), side_part(2)], axis=4)
    outer = lax.psum_scatter(outer, "gy", scatter_dimension=0, tiled=False)
    first = 2 * width
    from_up = lax.ppermute(outer[:, :, :, :first], "line", down)
    from_down = lax.ppermute(outer[:, :, :, first:], "line", up)
    result = lax.psum_scatter(side_part(1), "gy", scatter_dimension=0, tiled=False)
    result = result.at[:, :, :, width:].add(from_up)
    result = result.at[:, :, :, : 2 * width].add(from_down)
    result = jnp.transpose(result, (0, 3, 1, 2, 4))
    return result.reshape(shots, recv, 2, NF)


def grid_shape(mesh):
    row = mesh.devices[0]
    try:
        ys = sorted({d.coords[1] for d in row})
        zs = sorted({d.coords[2] for d in row})
        if len(ys) * len(zs) == len(row):
            return len(ys), len(zs)
    except Exception:
        pass
    return 4, len(row) // 4


def solution(mesh):
    rows, cols = grid_shape(mesh)
    lines = mesh.devices.shape[0]
    fine = Mesh(np.asarray(mesh.devices).reshape(lines, rows, cols), ("line", "gy", "gz"))
    split = ("line", "gy", "gz")
    mapped = jax.shard_map(
        body,
        mesh=fine,
        in_specs=(P(split, None, None), P(), P(split, None, None, None), P()),
        out_specs=P(split, None, None, None),
        check_vma=False,
    )
    out_sharding = NamedSharding(mesh, P(("line", "grp"), None, None, None))
    return jax.jit(mapped, out_shardings=out_sharding)
```

```python
import math

import jax
import jax.numpy as jnp
import numpy as np
from jax import lax
from jax.sharding import Mesh, NamedSharding
from jax.sharding import PartitionSpec as P

NF = 128
BP = 2
CAP = 16
RADIX = 64

HIGH = lax.Precision.HIGH


def dft_matrix(samples):
    inner = samples // RADIX
    major = jnp.arange(RADIX, dtype=jnp.int32)
    minor = jnp.arange(inner, dtype=jnp.int32)
    bins = jnp.arange(NF, dtype=jnp.int32)
    step = 2.0 * math.pi / samples
    angle_a = ((major[:, None] * inner * bins[None, :]) % samples).astype(jnp.float32) * step
    angle_n = ((minor[:, None] * bins[None, :]) % samples).astype(jnp.float32) * step
    a_re, a_im = jnp.cos(angle_a), -jnp.sin(angle_a)
    n_re, n_im = jnp.cos(angle_n), -jnp.sin(angle_n)
    scale = 1.0 / math.sqrt(samples)
    c_re = (a_re[:, None, :] * n_re[None, :, :] - a_im[:, None, :] * n_im[None, :, :]) * scale
    c_im = (a_re[:, None, :] * n_im[None, :, :] + a_im[:, None, :] * n_re[None, :, :]) * scale
    return jnp.concatenate([c_re, c_im], axis=-1).reshape(samples, 2 * NF)


def spectrum(traces, table):
    shots, recv, samples = traces.shape
    out = jnp.dot(traces.reshape(shots * recv, samples), table, precision=HIGH)
    return out.reshape(shots, recv // BP, BP, 2, NF)


def combine(cols, weight, block):
    w = weight[:, None, :, :, None, :, None]
    col_re = cols[:, :, :, :, None, 0, None, :]
    col_im = cols[:, :, :, :, None, 1, None, :]
    row_re = block[None, None, :, :, :, 0]
    row_im = block[None, None, :, :, :, 1]
    prod_re = -jnp.sum(w * (col_re * row_re - col_im * row_im), axis=(2, 3))
    prod_im = -jnp.sum(w * (col_re * row_im + col_im * row_re), axis=(2, 3))
    return jnp.stack([prod_re, prod_im], axis=3)


def body(shot_traces, aperture, taper_index, taper_table):
    line_count = lax.axis_size("line")
    rows = lax.axis_size("gy")
    cols = lax.axis_size("gz")
    my_line = lax.axis_index("line")
    my_row = lax.axis_index("gy")
    my_col = lax.axis_index("gz")
    shots, recv, samples = shot_traces.shape
    sides = 3
    width = recv // (BP * sides)
    blocks = sides * width
    up = [(i, (i + 1) % line_count) for i in range(line_count)]
    down = [((i + 1) % line_count, i) for i in range(line_count)]
    right = [(i, (i + 1) % cols) for i in range(cols)]
    left = [((i + 1) % cols, i) for i in range(cols)]
    spans = [(0, 2 * width), (0, blocks), (width, blocks)]

    taper_rows = taper_table.shape[0]
    pick = taper_index.reshape(sides, rows, cols, CAP)[..., None] == jnp.arange(taper_rows, dtype=jnp.int32)
    src_weight = jnp.sum(jnp.where(pick[..., None], taper_table, 0.0), axis=-2)
    own_blocks = lax.dynamic_slice_in_dim(aperture, (my_line * rows + my_row) * cols, cols, axis=0)
    slot_table = lax.dynamic_index_in_dim(
        own_blocks.reshape(cols, sides, rows, cols, CAP), my_col, 3, False
    )

    table = dft_matrix(samples)
    own = spectrum(shot_traces, table)

    stacked = own.reshape(shots, sides, rows, cols, BP, 2, NF)
    stacked = jnp.transpose(stacked, (1, 0, 2, 3, 4, 5, 6))
    spread = lax.all_to_all(stacked, "gy", split_axis=2, concat_axis=2, tiled=True)
    spread = jnp.transpose(spread, (0, 2, 1, 3, 4, 5, 6))
    side_cols = [
        lax.ppermute(spread[2], "line", up),
        spread[1],
        lax.ppermute(spread[0], "line", down),
    ]

    lanes = jnp.transpose(own, (0, 2, 3, 1, 4))
    half = blocks // 2
    ranges = [(0, half), (half, blocks)]

    def ring(payload):
        carried = [payload]
        offsets = [0]
        forward = payload
        backward = payload
        for step in range(1, cols // 2 + 1):
            forward = lax.ppermute(forward, "gz", right)
            carried.append(forward)
            offsets.append(-step)
            if 2 * step < cols:
                backward = lax.ppermute(backward, "gz", left)
                carried.append(backward)
                offsets.append(step)
        return carried, offsets

    pieces = [lanes[:, :, :, c0:c1] for c0, c1 in ranges]
    first_size = pieces[0].size
    carried, offsets = ring(jnp.concatenate([pieces[0].reshape(-1), src_weight.reshape(-1)]))
    sources = (my_col + jnp.asarray(offsets, dtype=jnp.int32)) % cols
    weights = jnp.stack([p[first_size:] for p in carried])
    weights = lax.dynamic_index_in_dim(
        weights.reshape((len(carried),) + src_weight.shape), my_col, 3, False
    )
    slots = jnp.take(slot_table, sources, axis=0)
    hit = slots[..., None] == jnp.arange(blocks, dtype=jnp.int32)
    dense = jnp.sum(jnp.where(hit[..., None], weights[:, :, :, :, None, :], 0.0), axis=3)
    dense = jnp.transpose(dense, (1, 2, 0, 4, 3))
    side_sel = [jnp.take(side_cols[s], sources, axis=2) for s in range(sides)]

    def half_part(c0, c1, piece, carried_c):
        gathered = jnp.stack([p.reshape(piece.shape) for p in carried_c])
        outs, lens = [], []
        for s in range(sides):
            r0, r1 = max(spans[s][0], c0), min(spans[s][1], c1)
            lens.append(max(r1 - r0, 0))
            if r0 < r1:
                outs.append(combine(side_sel[s], dense[s, :, :, :, r0:r1], gathered[:, :, :, :, r0 - c0:r1 - c0]))
        return jnp.concatenate(outs, axis=4), lens

    per_side = [[] for _ in range(sides)]

    def reduce_half(local, lens):
        reduced = lax.psum_scatter(local, "gy", scatter_dimension=0, tiled=False)
        at = 0
        for s in range(sides):
            if lens[s]:
                per_side[s].append(reduced[:, :, :, at:at + lens[s]])
                at += lens[s]

    local, lens = half_part(ranges[0][0], ranges[0][1], pieces[0], [p[:first_size] for p in carried])
    reduce_half(local, lens)
    second, _ = ring(pieces[1].reshape(-1) + 0.0 * local[0, 0, 0, 0, 0, 0])
    local, lens = half_part(ranges[1][0], ranges[1][1], pieces[1], second)
    reduce_half(local, lens)
    parts = [jnp.concatenate(p, axis=3) if len(p) > 1 else p[0] for p in per_side]

    from_up = lax.ppermute(parts[0], "line", down)
    from_down = lax.ppermute(parts[2], "line", up)
    result = parts[1]
    result = result.at[:, :, :, width:].add(from_up)
    result = result.at[:, :, :, : 2 * width].add(from_down)
    result = jnp.transpose(result, (0, 3, 1, 2, 4))
    return result.reshape(shots, recv, 2, NF)


def grid_shape(mesh):
    row = mesh.devices[0]
    try:
        ys = sorted({d.coords[1] for d in row})
        zs = sorted({d.coords[2] for d in row})
        if len(ys) * len(zs) == len(row):
            return len(ys), len(zs)
    except Exception:
        pass
    return 4, len(row) // 4


def solution(mesh):
    rows, cols = grid_shape(mesh)
    lines = mesh.devices.shape[0]
    fine = Mesh(np.asarray(mesh.devices).reshape(lines, rows, cols), ("line", "gy", "gz"))
    split = ("line", "gy", "gz")
    mapped = jax.shard_map(
        body,
        mesh=fine,
        in_specs=(P(split, None, None), P(), P(split, None, None, None), P()),
        out_specs=P(split, None, None, None),
        check_vma=False,
    )
    out_sharding = NamedSharding(mesh, P(("line", "grp"), None, None, None))
    return jax.jit(mapped, out_shardings=out_sharding)
```

```python
import math

import jax
import jax.numpy as jnp
import numpy as np
from jax import lax
from jax.sharding import Mesh, NamedSharding
from jax.sharding import PartitionSpec as P

NF = 128
BP = 2
CAP = 16
RADIX = 64

HIGH = lax.Precision.HIGH


def dft_matrix(samples):
    inner = samples // RADIX
    major = jnp.arange(RADIX, dtype=jnp.int32)
    minor = jnp.arange(inner, dtype=jnp.int32)
    bins = jnp.arange(NF, dtype=jnp.int32)
    step = 2.0 * math.pi / samples
    angle_a = ((major[:, None] * inner * bins[None, :]) % samples).astype(jnp.float32) * step
    angle_n = ((minor[:, None] * bins[None, :]) % samples).astype(jnp.float32) * step
    a_re, a_im = jnp.cos(angle_a), -jnp.sin(angle_a)
    n_re, n_im = jnp.cos(angle_n), -jnp.sin(angle_n)
    scale = 1.0 / math.sqrt(samples)
    c_re = (a_re[:, None, :] * n_re[None, :, :] - a_im[:, None, :] * n_im[None, :, :]) * scale
    c_im = (a_re[:, None, :] * n_im[None, :, :] + a_im[:, None, :] * n_re[None, :, :]) * scale
    return jnp.concatenate([c_re, c_im], axis=-1).reshape(samples, 2 * NF)


def spectrum(traces, table):
    shots, recv, samples = traces.shape
    out = jnp.dot(traces.reshape(shots * recv, samples), table, precision=HIGH)
    return out.reshape(shots, recv // BP, BP, 2, NF)


def combine(cols, weight, block):
    w = weight[:, None, :, :, None, :, None]
    col_re = cols[:, :, :, :, None, 0, None, :]
    col_im = cols[:, :, :, :, None, 1, None, :]
    row_re = block[None, None, :, :, :, 0]
    row_im = block[None, None, :, :, :, 1]
    prod_re = -jnp.sum(w * (col_re * row_re - col_im * row_im), axis=(2, 3))
    prod_im = -jnp.sum(w * (col_re * row_im + col_im * row_re), axis=(2, 3))
    return jnp.stack([prod_re, prod_im], axis=3)


def body(shot_traces, aperture, taper_index, taper_table):
    line_count = lax.axis_size("line")
    rows = lax.axis_size("gy")
    cols = lax.axis_size("gz")
    my_line = lax.axis_index("line")
    my_row = lax.axis_index("gy")
    my_col = lax.axis_index("gz")
    shots, recv, samples = shot_traces.shape
    sides = 3
    width = recv // (BP * sides)
    blocks = sides * width
    up = [(i, (i + 1) % line_count) for i in range(line_count)]
    down = [((i + 1) % line_count, i) for i in range(line_count)]
    right = [(i, (i + 1) % cols) for i in range(cols)]
    left = [((i + 1) % cols, i) for i in range(cols)]
    spans = [(0, 2 * width), (0, blocks), (width, blocks)]

    taper_rows = taper_table.shape[0]
    pick = taper_index.reshape(sides, rows, cols, CAP)[..., None] == jnp.arange(taper_rows, dtype=jnp.int32)
    src_weight = jnp.sum(jnp.where(pick[..., None], taper_table, 0.0), axis=-2)
    own_blocks = lax.dynamic_slice_in_dim(aperture, (my_line * rows + my_row) * cols, cols, axis=0)
    slot_table = lax.dynamic_index_in_dim(
        own_blocks.reshape(cols, sides, rows, cols, CAP), my_col, 3, False
    )

    table = dft_matrix(samples)
    own = spectrum(shot_traces, table)

    lanes = jnp.transpose(own, (0, 2, 3, 1, 4))
    spec_size = lanes.size
    payload = jnp.concatenate([lanes.reshape(-1), src_weight.reshape(-1)])
    carried = [payload]
    offsets = [0]
    forward = payload
    backward = payload
    for step in range(1, cols // 2 + 1):
        forward = lax.ppermute(forward, "gz", right)
        carried.append(forward)
        offsets.append(-step)
        if 2 * step < cols:
            backward = lax.ppermute(backward, "gz", left)
            carried.append(backward)
            offsets.append(step)
    first_arrival = carried[1][0]

    stacked = own.reshape(shots, sides, rows, cols, BP, 2, NF)
    stacked = jnp.transpose(stacked, (1, 0, 2, 3, 4, 5, 6))
    stacked = stacked + 0.0 * first_arrival
    spread = lax.all_to_all(stacked, "gy", split_axis=2, concat_axis=2, tiled=True)
    spread = jnp.transpose(spread, (0, 2, 1, 3, 4, 5, 6))
    side_cols = [
        lax.ppermute(spread[2], "line", up),
        spread[1],
        lax.ppermute(spread[0], "line", down),
    ]

    sources = (my_col + jnp.asarray(offsets, dtype=jnp.int32)) % cols
    ring = jnp.stack(carried)
    gathered = ring[:, :spec_size].reshape((len(carried),) + lanes.shape)
    weights = lax.dynamic_index_in_dim(
        ring[:, spec_size:].reshape((len(carried),) + src_weight.shape), my_col, 3, False
    )
    slots = jnp.take(slot_table, sources, axis=0)
    hit = slots[..., None] == jnp.arange(blocks, dtype=jnp.int32)
    dense = jnp.sum(jnp.where(hit[..., None], weights[:, :, :, :, None, :], 0.0), axis=3)
    dense = jnp.transpose(dense, (1, 2, 0, 4, 3))

    def side_part(s):
        lo, hi = spans[s]
        cols_s = jnp.take(side_cols[s], sources, axis=2)
        return combine(cols_s, dense[s, :, :, :, lo:hi], gathered[:, :, :, :, lo:hi])

    merged = jnp.concatenate([side_part(0), side_part(1), side_part(2)], axis=4)
    mine = lax.psum_scatter(merged, "gy", scatter_dimension=0, tiled=False)
    first, middle = 2 * width, 2 * width + blocks
    from_up = lax.ppermute(mine[:, :, :, :first], "line", down)
    from_down = lax.ppermute(mine[:, :, :, middle:], "line", up)
    result = mine[:, :, :, first:middle]
    result = result.at[:, :, :, width:].add(from_up)
    result = result.at[:, :, :, : 2 * width].add(from_down)
    result = jnp.transpose(result, (0, 3, 1, 2, 4))
    return result.reshape(shots, recv, 2, NF)


def grid_shape(mesh):
    row = mesh.devices[0]
    try:
        ys = sorted({d.coords[1] for d in row})
        zs = sorted({d.coords[2] for d in row})
        if len(ys) * len(zs) == len(row):
            return len(ys), len(zs)
    except Exception:
        pass
    return 4, len(row) // 4


def solution(mesh):
    rows, cols = grid_shape(mesh)
    lines = mesh.devices.shape[0]
    fine = Mesh(np.asarray(mesh.devices).reshape(lines, rows, cols), ("line", "gy", "gz"))
    split = ("line", "gy", "gz")
    mapped = jax.shard_map(
        body,
        mesh=fine,
        in_specs=(P(split, None, None), P(), P(split, None, None, None), P()),
        out_specs=P(split, None, None, None),
        check_vma=False,
    )
    out_sharding = NamedSharding(mesh, P(("line", "grp"), None, None, None))
    return jax.jit(mapped, out_shardings=out_sharding)
```

```python
import math

import jax
import jax.numpy as jnp
import numpy as np
from jax import lax
from jax.sharding import Mesh, NamedSharding
from jax.sharding import PartitionSpec as P

NF = 128
BP = 2
CAP = 16
RADIX = 64

HIGH = lax.Precision.HIGH


def dft_matrix(samples):
    inner = samples // RADIX
    major = jnp.arange(RADIX, dtype=jnp.int32)
    minor = jnp.arange(inner, dtype=jnp.int32)
    bins = jnp.arange(NF, dtype=jnp.int32)
    step = 2.0 * math.pi / samples
    angle_a = ((major[:, None] * inner * bins[None, :]) % samples).astype(jnp.float32) * step
    angle_n = ((minor[:, None] * bins[None, :]) % samples).astype(jnp.float32) * step
    a_re, a_im = jnp.cos(angle_a), -jnp.sin(angle_a)
    n_re, n_im = jnp.cos(angle_n), -jnp.sin(angle_n)
    scale = 1.0 / math.sqrt(samples)
    c_re = (a_re[:, None, :] * n_re[None, :, :] - a_im[:, None, :] * n_im[None, :, :]) * scale
    c_im = (a_re[:, None, :] * n_im[None, :, :] + a_im[:, None, :] * n_re[None, :, :]) * scale
    return jnp.concatenate([c_re, c_im], axis=-1).reshape(samples, 2 * NF)


def spectrum(traces, table):
    shots, recv, samples = traces.shape
    out = jnp.dot(traces.reshape(shots * recv, samples), table, precision=HIGH)
    return out.reshape(shots, recv // BP, BP, 2, NF)


def combine(cols, weight, block):
    w = weight[:, None, :, :, None, :, None]
    col_re = cols[:, :, :, :, None, 0, None, :]
    col_im = cols[:, :, :, :, None, 1, None, :]
    row_re = block[None, None, :, :, :, 0]
    row_im = block[None, None, :, :, :, 1]
    prod_re = -jnp.sum(w * (col_re * row_re - col_im * row_im), axis=(2, 3))
    prod_im = -jnp.sum(w * (col_re * row_im + col_im * row_re), axis=(2, 3))
    return jnp.stack([prod_re, prod_im], axis=3)


def body(shot_traces, aperture, taper_index, taper_table):
    line_count = lax.axis_size("line")
    rows = lax.axis_size("gy")
    cols = lax.axis_size("gz")
    my_line = lax.axis_index("line")
    my_row = lax.axis_index("gy")
    my_col = lax.axis_index("gz")
    shots, recv, samples = shot_traces.shape
    sides = 3
    width = recv // (BP * sides)
    blocks = sides * width
    up = [(i, (i + 1) % line_count) for i in range(line_count)]
    down = [((i + 1) % line_count, i) for i in range(line_count)]
    right = [(i, (i + 1) % cols) for i in range(cols)]
    left = [((i + 1) % cols, i) for i in range(cols)]
    spans = [(0, 2 * width), (0, blocks), (width, blocks)]

    taper_rows = taper_table.shape[0]
    pick = taper_index.reshape(sides, rows, cols, CAP)[..., None] == jnp.arange(taper_rows, dtype=jnp.int32)
    src_weight = jnp.sum(jnp.where(pick[..., None], taper_table, 0.0), axis=-2)
    own_blocks = lax.dynamic_slice_in_dim(aperture, (my_line * rows + my_row) * cols, cols, axis=0)
    slot_table = lax.dynamic_index_in_dim(
        own_blocks.reshape(cols, sides, rows, cols, CAP), my_col, 3, False
    )

    table = dft_matrix(samples)
    own = spectrum(shot_traces, table)

    lanes = jnp.transpose(own, (0, 2, 3, 1, 4))
    spec_size = lanes.size
    payload = jnp.concatenate([lanes.reshape(-1), src_weight.reshape(-1)])
    carried = [payload]
    offsets = [0]
    forward = payload
    backward = payload
    for step in range(1, cols // 2 + 1):
        forward = lax.ppermute(forward, "gz", right)
        carried.append(forward)
        offsets.append(-step)
        if 2 * step < cols:
            backward = lax.ppermute(backward, "gz", left)
            carried.append(backward)
            offsets.append(step)
    first_arrival = carried[-1][0] + carried[-2][0]

    stacked = own.reshape(shots, sides, rows, cols, BP, 2, NF)
    stacked = jnp.transpose(stacked, (1, 0, 2, 3, 4, 5, 6))
    stacked = stacked + 0.0 * first_arrival
    spread = lax.all_to_all(stacked, "gy", split_axis=2, concat_axis=2, tiled=True)
    spread = jnp.transpose(spread, (0, 2, 1, 3, 4, 5, 6))
    side_cols = [
        lax.ppermute(spread[2], "line", up),
        spread[1],
        lax.ppermute(spread[0], "line", down),
    ]

    sources = (my_col + jnp.asarray(offsets, dtype=jnp.int32)) % cols
    ring = jnp.stack(carried)
    gathered = ring[:, :spec_size].reshape((len(carried),) + lanes.shape)
    weights = lax.dynamic_index_in_dim(
        ring[:, spec_size:].reshape((len(carried),) + src_weight.shape), my_col, 3, False
    )
    slots = jnp.take(slot_table, sources, axis=0)
    hit = slots[..., None] == jnp.arange(blocks, dtype=jnp.int32)
    dense = jnp.sum(jnp.where(hit[..., None], weights[:, :, :, :, None, :], 0.0), axis=3)
    dense = jnp.transpose(dense, (1, 2, 0, 4, 3))

    def side_part(s):
        lo, hi = spans[s]
        cols_s = jnp.take(side_cols[s], sources, axis=2)
        return combine(cols_s, dense[s, :, :, :, lo:hi], gathered[:, :, :, :, lo:hi])

    merged = jnp.concatenate([side_part(0), side_part(1), side_part(2)], axis=4)
    mine = lax.psum_scatter(merged, "gy", scatter_dimension=0, tiled=False)
    first, middle = 2 * width, 2 * width + blocks
    from_up = lax.ppermute(mine[:, :, :, :first], "line", down)
    from_down = lax.ppermute(mine[:, :, :, middle:], "line", up)
    result = mine[:, :, :, first:middle]
    result = result.at[:, :, :, width:].add(from_up)
    result = result.at[:, :, :, : 2 * width].add(from_down)
    result = jnp.transpose(result, (0, 3, 1, 2, 4))
    return result.reshape(shots, recv, 2, NF)


def grid_shape(mesh):
    row = mesh.devices[0]
    try:
        ys = sorted({d.coords[1] for d in row})
        zs = sorted({d.coords[2] for d in row})
        if len(ys) * len(zs) == len(row):
            return len(ys), len(zs)
    except Exception:
        pass
    return 4, len(row) // 4


def solution(mesh):
    rows, cols = grid_shape(mesh)
    lines = mesh.devices.shape[0]
    fine = Mesh(np.asarray(mesh.devices).reshape(lines, rows, cols), ("line", "gy", "gz"))
    split = ("line", "gy", "gz")
    mapped = jax.shard_map(
        body,
        mesh=fine,
        in_specs=(P(split, None, None), P(), P(split, None, None, None), P()),
        out_specs=P(split, None, None, None),
        check_vma=False,
    )
    out_sharding = NamedSharding(mesh, P(("line", "grp"), None, None, None))
    return jax.jit(mapped, out_shardings=out_sharding)
```

```python
import math

import jax
import jax.numpy as jnp
import numpy as np
from jax import lax
from jax.sharding import Mesh, NamedSharding
from jax.sharding import PartitionSpec as P

NF = 128
BP = 2
CAP = 16
RADIX = 64

HIGH = lax.Precision.HIGH


def dft_matrix(samples):
    inner = samples // RADIX
    major = jnp.arange(RADIX, dtype=jnp.int32)
    minor = jnp.arange(inner, dtype=jnp.int32)
    bins = jnp.arange(NF, dtype=jnp.int32)
    step = 2.0 * math.pi / samples
    angle_a = ((major[:, None] * inner * bins[None, :]) % samples).astype(jnp.float32) * step
    angle_n = ((minor[:, None] * bins[None, :]) % samples).astype(jnp.float32) * step
    a_re, a_im = jnp.cos(angle_a), -jnp.sin(angle_a)
    n_re, n_im = jnp.cos(angle_n), -jnp.sin(angle_n)
    scale = 1.0 / math.sqrt(samples)
    c_re = (a_re[:, None, :] * n_re[None, :, :] - a_im[:, None, :] * n_im[None, :, :]) * scale
    c_im = (a_re[:, None, :] * n_im[None, :, :] + a_im[:, None, :] * n_re[None, :, :]) * scale
    return jnp.concatenate([c_re, c_im], axis=-1).reshape(samples, 2 * NF)


def spectrum(traces, table):
    shots, recv, samples = traces.shape
    out = jnp.dot(traces.reshape(shots * recv, samples), table, precision=HIGH)
    return out.reshape(shots, recv // BP, BP, 2, NF)


def combine(cols, weight, block):
    w = weight[:, None, :, :, None, :, None]
    col_re = cols[:, :, :, :, None, 0, None, :]
    col_im = cols[:, :, :, :, None, 1, None, :]
    row_re = block[None, None, :, :, :, 0]
    row_im = block[None, None, :, :, :, 1]
    prod_re = -jnp.sum(w * (col_re * row_re - col_im * row_im), axis=(2, 3))
    prod_im = -jnp.sum(w * (col_re * row_im + col_im * row_re), axis=(2, 3))
    return jnp.stack([prod_re, prod_im], axis=3)


def body(shot_traces, aperture, taper_index, taper_table):
    line_count = lax.axis_size("line")
    rows = lax.axis_size("gy")
    cols = lax.axis_size("gz")
    my_line = lax.axis_index("line")
    my_row = lax.axis_index("gy")
    my_col = lax.axis_index("gz")
    shots, recv, samples = shot_traces.shape
    sides = 3
    width = recv // (BP * sides)
    blocks = sides * width
    up = [(i, (i + 1) % line_count) for i in range(line_count)]
    down = [((i + 1) % line_count, i) for i in range(line_count)]
    right = [(i, (i + 1) % cols) for i in range(cols)]
    left = [((i + 1) % cols, i) for i in range(cols)]
    spans = [(0, 2 * width), (0, blocks), (width, blocks)]

    taper_rows = taper_table.shape[0]
    pick = taper_index.reshape(sides, rows, cols, CAP)[..., None] == jnp.arange(taper_rows, dtype=jnp.int32)
    src_weight = jnp.sum(jnp.where(pick[..., None], taper_table, 0.0), axis=-2)
    own_blocks = lax.dynamic_slice_in_dim(aperture, (my_line * rows + my_row) * cols, cols, axis=0)
    slot_table = lax.dynamic_index_in_dim(
        own_blocks.reshape(cols, sides, rows, cols, CAP), my_col, 3, False
    )

    table = dft_matrix(samples)
    own = spectrum(shot_traces, table)

    stacked = own.reshape(shots, sides, rows, cols, BP, 2, NF)
    stacked = jnp.transpose(stacked, (1, 0, 2, 3, 4, 5, 6))
    spread = lax.all_to_all(stacked, "gy", split_axis=2, concat_axis=2, tiled=True)
    spread = jnp.transpose(spread, (0, 2, 1, 3, 4, 5, 6))
    side_cols = [
        lax.ppermute(spread[2], "line", up),
        spread[1],
        lax.ppermute(spread[0], "line", down),
    ]

    lanes = jnp.transpose(own, (0, 2, 3, 1, 4))
    spec_rows = lanes.size // NF
    payload = jnp.concatenate([lanes.reshape(spec_rows, NF), src_weight.reshape(-1, NF)], axis=0)
    carried = [payload]
    offsets = [0]
    forward = payload
    backward = payload
    split = payload.shape[0] // 16 * 8
    for step in range(1, cols // 2 + 1):
        if 2 * step == cols:
            head = lax.ppermute(forward[:split], "gz", right)
            tail = lax.ppermute(backward[split:], "gz", left)
            carried.append(jnp.concatenate([head, tail], axis=0))
            offsets.append(step)
            break
        forward = lax.ppermute(forward, "gz", right)
        carried.append(forward)
        offsets.append(-step)
        backward = lax.ppermute(backward, "gz", left)
        carried.append(backward)
        offsets.append(step)
    sources = (my_col + jnp.asarray(offsets, dtype=jnp.int32)) % cols
    ring = jnp.stack(carried)
    gathered = ring[:, :spec_rows].reshape((len(carried),) + lanes.shape)
    weights = lax.dynamic_index_in_dim(
        ring[:, spec_rows:].reshape((len(carried),) + src_weight.shape), my_col, 3, False
    )
    slots = jnp.take(slot_table, sources, axis=0)
    hit = slots[..., None] == jnp.arange(blocks, dtype=jnp.int32)
    dense = jnp.sum(jnp.where(hit[..., None], weights[:, :, :, :, None, :], 0.0), axis=3)
    dense = jnp.transpose(dense, (1, 2, 0, 4, 3))

    def side_part(s):
        lo, hi = spans[s]
        cols_s = jnp.take(side_cols[s], sources, axis=2)
        return combine(cols_s, dense[s, :, :, :, lo:hi], gathered[:, :, :, :, lo:hi])

    outer = jnp.concatenate([side_part(0), side_part(2)], axis=4)
    outer = lax.psum_scatter(outer, "gy", scatter_dimension=0, tiled=False)
    first = 2 * width
    from_up = lax.ppermute(outer[:, :, :, :first], "line", down)
    from_down = lax.ppermute(outer[:, :, :, first:], "line", up)
    result = lax.psum_scatter(side_part(1), "gy", scatter_dimension=0, tiled=False)
    result = result.at[:, :, :, width:].add(from_up)
    result = result.at[:, :, :, : 2 * width].add(from_down)
    result = jnp.transpose(result, (0, 3, 1, 2, 4))
    return result.reshape(shots, recv, 2, NF)


def grid_shape(mesh):
    row = mesh.devices[0]
    try:
        ys = sorted({d.coords[1] for d in row})
        zs = sorted({d.coords[2] for d in row})
        if len(ys) * len(zs) == len(row):
            return len(ys), len(zs)
    except Exception:
        pass
    return 4, len(row) // 4


def solution(mesh):
    rows, cols = grid_shape(mesh)
    lines = mesh.devices.shape[0]
    fine = Mesh(np.asarray(mesh.devices).reshape(lines, rows, cols), ("line", "gy", "gz"))
    split = ("line", "gy", "gz")
    mapped = jax.shard_map(
        body,
        mesh=fine,
        in_specs=(P(split, None, None), P(), P(split, None, None, None), P()),
        out_specs=P(split, None, None, None),
        check_vma=False,
    )
    out_sharding = NamedSharding(mesh, P(("line", "grp"), None, None, None))
    return jax.jit(mapped, out_shardings=out_sharding)
```

```python
import math

import jax
import jax.numpy as jnp
import numpy as np
from jax import lax
from jax.sharding import Mesh, NamedSharding
from jax.sharding import PartitionSpec as P

NF = 128
BP = 2
CAP = 16
RADIX = 64

HIGH = lax.Precision.HIGH


def dft_matrix(samples):
    inner = samples // RADIX
    major = jnp.arange(RADIX, dtype=jnp.int32)
    minor = jnp.arange(inner, dtype=jnp.int32)
    bins = jnp.arange(NF, dtype=jnp.int32)
    step = 2.0 * math.pi / samples
    angle_a = ((major[:, None] * inner * bins[None, :]) % samples).astype(jnp.float32) * step
    angle_n = ((minor[:, None] * bins[None, :]) % samples).astype(jnp.float32) * step
    a_re, a_im = jnp.cos(angle_a), -jnp.sin(angle_a)
    n_re, n_im = jnp.cos(angle_n), -jnp.sin(angle_n)
    scale = 1.0 / math.sqrt(samples)
    c_re = (a_re[:, None, :] * n_re[None, :, :] - a_im[:, None, :] * n_im[None, :, :]) * scale
    c_im = (a_re[:, None, :] * n_im[None, :, :] + a_im[:, None, :] * n_re[None, :, :]) * scale
    return jnp.concatenate([c_re, c_im], axis=-1).reshape(samples, 2 * NF)


def spectrum(traces, table):
    shots, recv, samples = traces.shape
    out = jnp.dot(traces.reshape(shots * recv, samples), table, precision=HIGH)
    return out.reshape(shots, recv // BP, BP, 2, NF)


def combine(cols, weight, block):
    w = weight[:, None, :, :, None, :, None]
    col_re = cols[:, :, :, :, None, 0, None, :]
    col_im = cols[:, :, :, :, None, 1, None, :]
    row_re = block[None, None, :, :, :, 0]
    row_im = block[None, None, :, :, :, 1]
    prod_re = -jnp.sum(w * (col_re * row_re - col_im * row_im), axis=(2, 3))
    prod_im = -jnp.sum(w * (col_re * row_im + col_im * row_re), axis=(2, 3))
    return jnp.stack([prod_re, prod_im], axis=3)


def body(shot_traces, aperture, taper_index, taper_table):
    line_count = lax.axis_size("line")
    rows = lax.axis_size("gy")
    cols = lax.axis_size("gz")
    my_line = lax.axis_index("line")
    my_row = lax.axis_index("gy")
    my_col = lax.axis_index("gz")
    shots, recv, samples = shot_traces.shape
    sides = 3
    width = recv // (BP * sides)
    blocks = sides * width
    up = [(i, (i + 1) % line_count) for i in range(line_count)]
    down = [((i + 1) % line_count, i) for i in range(line_count)]
    right = [(i, (i + 1) % cols) for i in range(cols)]
    left = [((i + 1) % cols, i) for i in range(cols)]
    spans = [(0, 2 * width), (0, blocks), (width, blocks)]

    taper_rows = taper_table.shape[0]
    pick = taper_index.reshape(sides, rows, cols, CAP)[..., None] == jnp.arange(taper_rows, dtype=jnp.int32)
    src_weight = jnp.sum(jnp.where(pick[..., None], taper_table, 0.0), axis=-2)
    own_blocks = lax.dynamic_slice_in_dim(aperture, (my_line * rows + my_row) * cols, cols, axis=0)
    slot_table = lax.dynamic_index_in_dim(
        own_blocks.reshape(cols, sides, rows, cols, CAP), my_col, 3, False
    )

    table = dft_matrix(samples)
    own = spectrum(shot_traces, table)

    stacked = own.reshape(shots, sides, rows, cols, BP, 2, NF)
    stacked = jnp.transpose(stacked, (1, 0, 2, 3, 4, 5, 6))
    spread = lax.all_to_all(stacked, "gy", split_axis=2, concat_axis=2, tiled=True)
    spread = jnp.transpose(spread, (0, 2, 1, 3, 4, 5, 6))
    side_cols = [
        lax.ppermute(spread[2], "line", up),
        spread[1],
        lax.ppermute(spread[0], "line", down),
    ]

    lanes = jnp.transpose(own, (0, 2, 3, 1, 4))
    spec_rows = lanes.size // NF
    payload = jnp.concatenate([lanes.reshape(spec_rows, NF), src_weight.reshape(-1, NF)], axis=0)
    carried = [payload]
    offsets = [0]
    forward = payload
    backward = payload
    split = payload.shape[0] // 16 * 8
    for step in range(1, cols // 2 + 1):
        if 2 * step == cols:
            head = lax.ppermute(forward[:split], "gz", right)
            tail = lax.ppermute(backward[split:], "gz", left)
            carried.append(jnp.concatenate([head, tail], axis=0))
            offsets.append(step)
            break
        forward = lax.ppermute(forward, "gz", right)
        carried.append(forward)
        offsets.append(-step)
        backward = lax.ppermute(backward, "gz", left)
        carried.append(backward)
        offsets.append(step)
    sources = (my_col + jnp.asarray(offsets, dtype=jnp.int32)) % cols
    ring = jnp.stack(carried)
    gathered = ring[:, :spec_rows].reshape((len(carried),) + lanes.shape)
    weights = lax.dynamic_index_in_dim(
        ring[:, spec_rows:].reshape((len(carried),) + src_weight.shape), my_col, 3, False
    )
    slots = jnp.take(slot_table, sources, axis=0)
    hit = slots[..., None] == jnp.arange(blocks, dtype=jnp.int32)
    dense = jnp.sum(jnp.where(hit[..., None], weights[:, :, :, :, None, :], 0.0), axis=3)
    dense = jnp.transpose(dense, (1, 2, 0, 4, 3))

    def side_part(s):
        lo, hi = spans[s]
        cols_s = jnp.take(side_cols[s], sources, axis=2)
        return combine(cols_s, dense[s, :, :, :, lo:hi], gathered[:, :, :, :, lo:hi])

    merged = jnp.concatenate([side_part(0), side_part(1), side_part(2)], axis=4)
    mine = lax.psum_scatter(merged, "gy", scatter_dimension=0, tiled=False)
    first, middle = 2 * width, 2 * width + blocks
    from_up = lax.ppermute(mine[:, :, :, :first], "line", down)
    from_down = lax.ppermute(mine[:, :, :, middle:], "line", up)
    result = mine[:, :, :, first:middle]
    result = result.at[:, :, :, width:].add(from_up)
    result = result.at[:, :, :, : 2 * width].add(from_down)
    result = jnp.transpose(result, (0, 3, 1, 2, 4))
    return result.reshape(shots, recv, 2, NF)


def grid_shape(mesh):
    row = mesh.devices[0]
    try:
        ys = sorted({d.coords[1] for d in row})
        zs = sorted({d.coords[2] for d in row})
        if len(ys) * len(zs) == len(row):
            return len(ys), len(zs)
    except Exception:
        pass
    return 4, len(row) // 4


def solution(mesh):
    rows, cols = grid_shape(mesh)
    lines = mesh.devices.shape[0]
    fine = Mesh(np.asarray(mesh.devices).reshape(lines, rows, cols), ("line", "gy", "gz"))
    split = ("line", "gy", "gz")
    mapped = jax.shard_map(
        body,
        mesh=fine,
        in_specs=(P(split, None, None), P(), P(split, None, None, None), P()),
        out_specs=P(split, None, None, None),
        check_vma=False,
    )
    out_sharding = NamedSharding(mesh, P(("line", "grp"), None, None, None))
    return jax.jit(mapped, out_shardings=out_sharding)
```

```python
import math

import jax
import jax.numpy as jnp
import numpy as np
from jax import lax
from jax.sharding import Mesh, NamedSharding
from jax.sharding import PartitionSpec as P

NF = 128
BP = 2
CAP = 16
RADIX = 64

HIGH = lax.Precision.HIGH


def dft_matrix(samples):
    inner = samples // RADIX
    major = jnp.arange(RADIX, dtype=jnp.int32)
    minor = jnp.arange(inner, dtype=jnp.int32)
    bins = jnp.arange(NF, dtype=jnp.int32)
    step = 2.0 * math.pi / samples
    angle_a = ((major[:, None] * inner * bins[None, :]) % samples).astype(jnp.float32) * step
    angle_n = ((minor[:, None] * bins[None, :]) % samples).astype(jnp.float32) * step
    a_re, a_im = jnp.cos(angle_a), -jnp.sin(angle_a)
    n_re, n_im = jnp.cos(angle_n), -jnp.sin(angle_n)
    scale = 1.0 / math.sqrt(samples)
    c_re = (a_re[:, None, :] * n_re[None, :, :] - a_im[:, None, :] * n_im[None, :, :]) * scale
    c_im = (a_re[:, None, :] * n_im[None, :, :] + a_im[:, None, :] * n_re[None, :, :]) * scale
    return jnp.concatenate([c_re, c_im], axis=-1).reshape(samples, 2 * NF)


def spectrum(traces, table):
    shots, recv, samples = traces.shape
    out = jnp.dot(traces.reshape(shots * recv, samples), table, precision=HIGH)
    return out.reshape(shots, recv // BP, BP, 2, NF)


def combine(cols, weight, block):
    w = weight[:, None, :, :, None, :, None]
    col_re = cols[:, :, :, :, None, 0, None, :]
    col_im = cols[:, :, :, :, None, 1, None, :]
    row_re = block[None, None, :, :, :, 0]
    row_im = block[None, None, :, :, :, 1]
    prod_re = -jnp.sum(w * (col_re * row_re - col_im * row_im), axis=(2, 3))
    prod_im = -jnp.sum(w * (col_re * row_im + col_im * row_re), axis=(2, 3))
    return jnp.stack([prod_re, prod_im], axis=3)


def body(shot_traces, aperture, taper_index, taper_table):
    line_count = lax.axis_size("line")
    rows = lax.axis_size("gy")
    cols = lax.axis_size("gz")
    my_line = lax.axis_index("line")
    my_row = lax.axis_index("gy")
    my_col = lax.axis_index("gz")
    shots, recv, samples = shot_traces.shape
    sides = 3
    width = recv // (BP * sides)
    blocks = sides * width
    up = [(i, (i + 1) % line_count) for i in range(line_count)]
    down = [((i + 1) % line_count, i) for i in range(line_count)]
    right = [(i, (i + 1) % cols) for i in range(cols)]
    left = [((i + 1) % cols, i) for i in range(cols)]
    spans = [(0, 2 * width), (0, blocks), (width, blocks)]

    taper_rows = taper_table.shape[0]
    pick = taper_index.reshape(sides, rows, cols, CAP)[..., None] == jnp.arange(taper_rows, dtype=jnp.int32)
    src_weight = jnp.sum(jnp.where(pick[..., None], taper_table, 0.0), axis=-2)
    own_blocks = lax.dynamic_slice_in_dim(aperture, (my_line * rows + my_row) * cols, cols, axis=0)
    slot_table = lax.dynamic_index_in_dim(
        own_blocks.reshape(cols, sides, rows, cols, CAP), my_col, 3, False
    )

    table = dft_matrix(samples)
    own = spectrum(shot_traces, table)

    stacked = own.reshape(shots, sides, rows, cols, BP, 2, NF)
    stacked = jnp.transpose(stacked, (1, 0, 2, 3, 4, 5, 6))
    spread = lax.all_to_all(stacked, "gy", split_axis=2, concat_axis=2, tiled=True)
    spread = jnp.transpose(spread, (0, 2, 1, 3, 4, 5, 6))
    side_cols = [
        lax.ppermute(spread[2], "line", up),
        spread[1],
        lax.ppermute(spread[0], "line", down),
    ]

    lanes = jnp.transpose(own, (0, 2, 3, 1, 4))
    spec_rows = lanes.size // NF
    payload = jnp.concatenate([lanes.reshape(spec_rows, NF), src_weight.reshape(-1, NF)], axis=0)
    carried = [payload]
    offsets = [0]
    forward = payload
    backward = payload
    split = payload.shape[0] // 16 * 8
    for step in range(1, cols // 2 + 1):
        if 2 * step == cols:
            head = lax.ppermute(forward[:split], "gz", right)
            tail = lax.ppermute(backward[split:], "gz", left)
            carried.append(jnp.concatenate([head, tail], axis=0))
            offsets.append(step)
            break
        forward = lax.ppermute(forward, "gz", right)
        carried.append(forward)
        offsets.append(-step)
        backward = lax.ppermute(backward, "gz", left)
        carried.append(backward)
        offsets.append(step)
    sources = (my_col + jnp.asarray(offsets, dtype=jnp.int32)) % cols
    ring = jnp.stack(carried)
    gathered = ring[:, :spec_rows].reshape((len(carried),) + lanes.shape)
    weights = lax.dynamic_index_in_dim(
        ring[:, spec_rows:].reshape((len(carried),) + src_weight.shape), my_col, 3, False
    )
    slots = jnp.take(slot_table, sources, axis=0)
    hit = slots[..., None] == jnp.arange(blocks, dtype=jnp.int32)
    dense = jnp.sum(jnp.where(hit[..., None], weights[:, :, :, :, None, :], 0.0), axis=3)
    dense = jnp.transpose(dense, (1, 2, 0, 4, 3))

    def side_part(s):
        lo, hi = spans[s]
        cols_s = jnp.take(side_cols[s], sources, axis=2)
        return combine(cols_s, dense[s, :, :, :, lo:hi], gathered[:, :, :, :, lo:hi])

    from_up = lax.ppermute(side_part(0), "line", down)
    from_down = lax.ppermute(side_part(2), "line", up)
    total = side_part(1)
    total = total.at[:, :, :, :, width:].add(from_up)
    total = total.at[:, :, :, :, : 2 * width].add(from_down)
    result = lax.psum_scatter(total, "gy", scatter_dimension=0, tiled=False)
    result = jnp.transpose(result, (0, 3, 1, 2, 4))
    return result.reshape(shots, recv, 2, NF)


def grid_shape(mesh):
    row = mesh.devices[0]
    try:
        ys = sorted({d.coords[1] for d in row})
        zs = sorted({d.coords[2] for d in row})
        if len(ys) * len(zs) == len(row):
            return len(ys), len(zs)
    except Exception:
        pass
    return 4, len(row) // 4


def solution(mesh):
    rows, cols = grid_shape(mesh)
    lines = mesh.devices.shape[0]
    fine = Mesh(np.asarray(mesh.devices).reshape(lines, rows, cols), ("line", "gy", "gz"))
    split = ("line", "gy", "gz")
    mapped = jax.shard_map(
        body,
        mesh=fine,
        in_specs=(P(split, None, None), P(), P(split, None, None, None), P()),
        out_specs=P(split, None, None, None),
        check_vma=False,
    )
    out_sharding = NamedSharding(mesh, P(("line", "grp"), None, None, None))
    return jax.jit(mapped, out_shardings=out_sharding)
```

```python
import math

import jax
import jax.numpy as jnp
import numpy as np
from jax import lax
from jax.sharding import Mesh, NamedSharding
from jax.sharding import PartitionSpec as P

NF = 128
BP = 2
CAP = 16
RADIX = 64

HIGH = lax.Precision.HIGH


def dft_matrix(samples):
    inner = samples // RADIX
    major = jnp.arange(RADIX, dtype=jnp.int32)
    minor = jnp.arange(inner, dtype=jnp.int32)
    bins = jnp.arange(NF, dtype=jnp.int32)
    step = 2.0 * math.pi / samples
    angle_a = ((major[:, None] * inner * bins[None, :]) % samples).astype(jnp.float32) * step
    angle_n = ((minor[:, None] * bins[None, :]) % samples).astype(jnp.float32) * step
    a_re, a_im = jnp.cos(angle_a), -jnp.sin(angle_a)
    n_re, n_im = jnp.cos(angle_n), -jnp.sin(angle_n)
    scale = 1.0 / math.sqrt(samples)
    c_re = (a_re[:, None, :] * n_re[None, :, :] - a_im[:, None, :] * n_im[None, :, :]) * scale
    c_im = (a_re[:, None, :] * n_im[None, :, :] + a_im[:, None, :] * n_re[None, :, :]) * scale
    return jnp.concatenate([c_re, c_im], axis=-1).reshape(samples, 2 * NF)


def spectrum(traces, table):
    shots, recv, samples = traces.shape
    out = jnp.dot(traces.reshape(shots * recv, samples), table, precision=HIGH)
    return out.reshape(shots, recv // BP, BP, 2, NF)


def combine(cols, weight, block):
    w = weight[:, None, :, :, None, :, None]
    col_re = cols[:, :, :, :, None, 0, None, :]
    col_im = cols[:, :, :, :, None, 1, None, :]
    row_re = block[None, None, :, :, :, 0]
    row_im = block[None, None, :, :, :, 1]
    prod_re = -jnp.sum(w * (col_re * row_re - col_im * row_im), axis=(2, 3))
    prod_im = -jnp.sum(w * (col_re * row_im + col_im * row_re), axis=(2, 3))
    return jnp.stack([prod_re, prod_im], axis=3)


def body(shot_traces, aperture, taper_index, taper_table):
    line_count = lax.axis_size("line")
    rows = lax.axis_size("gy")
    cols = lax.axis_size("gz")
    my_line = lax.axis_index("line")
    my_row = lax.axis_index("gy")
    my_col = lax.axis_index("gz")
    shots, recv, samples = shot_traces.shape
    sides = 3
    width = recv // (BP * sides)
    blocks = sides * width
    up = [(i, (i + 1) % line_count) for i in range(line_count)]
    down = [((i + 1) % line_count, i) for i in range(line_count)]
    right = [(i, (i + 1) % cols) for i in range(cols)]
    left = [((i + 1) % cols, i) for i in range(cols)]
    spans = [(0, 2 * width), (0, blocks), (width, blocks)]

    taper_rows = taper_table.shape[0]
    pick = taper_index.reshape(sides, rows, cols, CAP)[..., None] == jnp.arange(taper_rows, dtype=jnp.int32)
    src_weight = jnp.sum(jnp.where(pick[..., None], taper_table, 0.0), axis=-2)
    own_blocks = lax.dynamic_slice_in_dim(aperture, (my_line * rows + my_row) * cols, cols, axis=0)
    slot_table = lax.dynamic_index_in_dim(
        own_blocks.reshape(cols, sides, rows, cols, CAP), my_col, 3, False
    )

    table = dft_matrix(samples)
    own = spectrum(shot_traces, table)

    stacked = own.reshape(shots, sides, rows, cols, BP, 2, NF)
    stacked = jnp.transpose(stacked, (1, 0, 2, 3, 4, 5, 6))
    spread = lax.all_to_all(stacked, "gy", split_axis=2, concat_axis=2, tiled=True)
    spread = jnp.transpose(spread, (0, 2, 1, 3, 4, 5, 6))
    side_cols = [
        lax.ppermute(spread[2], "line", up),
        spread[1],
        lax.ppermute(spread[0], "line", down),
    ]

    lanes = jnp.transpose(own, (0, 2, 3, 1, 4))
    spec_rows = lanes.size // NF
    payload = jnp.concatenate([lanes.reshape(spec_rows, NF), src_weight.reshape(-1, NF)], axis=0)
    carried = [payload]
    offsets = [0]
    forward = payload
    backward = payload
    split = payload.shape[0] // 16 * 8
    for step in range(1, cols // 2 + 1):
        if 2 * step == cols:
            head = lax.ppermute(forward[:split], "gz", right)
            tail = lax.ppermute(backward[split:], "gz", left)
            carried.append(jnp.concatenate([head, tail], axis=0))
            offsets.append(step)
            break
        forward = lax.ppermute(forward, "gz", right)
        carried.append(forward)
        offsets.append(-step)
        backward = lax.ppermute(backward, "gz", left)
        carried.append(backward)
        offsets.append(step)
    sources = (my_col + jnp.asarray(offsets, dtype=jnp.int32)) % cols
    ring = jnp.stack(carried)
    gathered = ring[:, :spec_rows].reshape((len(carried),) + lanes.shape)
    weights = lax.dynamic_index_in_dim(
        ring[:, spec_rows:].reshape((len(carried),) + src_weight.shape), my_col, 3, False
    )
    slots = jnp.take(slot_table, sources, axis=0)
    hit = slots[..., None] == jnp.arange(blocks, dtype=jnp.int32)
    dense = jnp.sum(jnp.where(hit[..., None], weights[:, :, :, :, None, :], 0.0), axis=3)
    dense = jnp.transpose(dense, (1, 2, 0, 4, 3))

    def side_part(s):
        cols_s = jnp.take(side_cols[s], sources, axis=2)
        lo, hi = spans[s]
        return combine(cols_s, dense[s], gathered)[:, :, :, :, lo:hi]

    from_up = lax.ppermute(side_part(0), "line", down)
    from_down = lax.ppermute(side_part(2), "line", up)
    total = side_part(1)
    total = total.at[:, :, :, :, width:].add(from_up)
    total = total.at[:, :, :, :, : 2 * width].add(from_down)
    result = lax.psum_scatter(total, "gy", scatter_dimension=0, tiled=False)
    result = jnp.transpose(result, (0, 3, 1, 2, 4))
    return result.reshape(shots, recv, 2, NF)


def grid_shape(mesh):
    row = mesh.devices[0]
    try:
        ys = sorted({d.coords[1] for d in row})
        zs = sorted({d.coords[2] for d in row})
        if len(ys) * len(zs) == len(row):
            return len(ys), len(zs)
    except Exception:
        pass
    return 4, len(row) // 4


def solution(mesh):
    rows, cols = grid_shape(mesh)
    lines = mesh.devices.shape[0]
    fine = Mesh(np.asarray(mesh.devices).reshape(lines, rows, cols), ("line", "gy", "gz"))
    split = ("line", "gy", "gz")
    mapped = jax.shard_map(
        body,
        mesh=fine,
        in_specs=(P(split, None, None), P(), P(split, None, None, None), P()),
        out_specs=P(split, None, None, None),
        check_vma=False,
    )
    out_sharding = NamedSharding(mesh, P(("line", "grp"), None, None, None))
    return jax.jit(mapped, out_shardings=out_sharding)
```

```python
import math

import jax
import jax.numpy as jnp
import numpy as np
from jax import lax
from jax.sharding import Mesh, NamedSharding
from jax.sharding import PartitionSpec as P

NF = 128
BP = 2
CAP = 16
RADIX = 64

HIGH = lax.Precision.HIGH


def dft_matrix(samples):
    inner = samples // RADIX
    major = jnp.arange(RADIX, dtype=jnp.int32)
    minor = jnp.arange(inner, dtype=jnp.int32)
    bins = jnp.arange(NF, dtype=jnp.int32)
    step = 2.0 * math.pi / samples
    angle_a = ((major[:, None] * inner * bins[None, :]) % samples).astype(jnp.float32) * step
    angle_n = ((minor[:, None] * bins[None, :]) % samples).astype(jnp.float32) * step
    a_re, a_im = jnp.cos(angle_a), -jnp.sin(angle_a)
    n_re, n_im = jnp.cos(angle_n), -jnp.sin(angle_n)
    scale = 1.0 / math.sqrt(samples)
    c_re = (a_re[:, None, :] * n_re[None, :, :] - a_im[:, None, :] * n_im[None, :, :]) * scale
    c_im = (a_re[:, None, :] * n_im[None, :, :] + a_im[:, None, :] * n_re[None, :, :]) * scale
    return jnp.concatenate([c_re, c_im], axis=-1).reshape(samples, 2 * NF)


def spectrum(traces, table):
    shots, recv, samples = traces.shape
    out = jnp.dot(traces.reshape(shots * recv, samples), table, precision=HIGH)
    return out.reshape(shots, recv // BP, BP, 2, NF)


def combine(cols, weight, block):
    w = weight[:, None, :, :, None, :, None]
    col_re = cols[:, :, :, :, None, 0, None, :]
    col_im = cols[:, :, :, :, None, 1, None, :]
    row_re = block[None, None, :, :, :, 0]
    row_im = block[None, None, :, :, :, 1]
    prod_re = -jnp.sum(w * (col_re * row_re - col_im * row_im), axis=(2, 3))
    prod_im = -jnp.sum(w * (col_re * row_im + col_im * row_re), axis=(2, 3))
    return jnp.stack([prod_re, prod_im], axis=3)


def body(shot_traces, aperture, taper_index, taper_table):
    line_count = lax.axis_size("line")
    rows = lax.axis_size("gy")
    cols = lax.axis_size("gz")
    my_line = lax.axis_index("line")
    my_row = lax.axis_index("gy")
    my_col = lax.axis_index("gz")
    shots, recv, samples = shot_traces.shape
    sides = 3
    width = recv // (BP * sides)
    blocks = sides * width
    up = [(i, (i + 1) % line_count) for i in range(line_count)]
    down = [((i + 1) % line_count, i) for i in range(line_count)]
    right = [(i, (i + 1) % cols) for i in range(cols)]
    left = [((i + 1) % cols, i) for i in range(cols)]
    spans = [(0, 2 * width), (0, blocks), (width, blocks)]

    taper_rows = taper_table.shape[0]
    pick = taper_index.reshape(sides, rows, cols, CAP)[..., None] == jnp.arange(taper_rows, dtype=jnp.int32)
    src_weight = jnp.sum(jnp.where(pick[..., None], taper_table, 0.0), axis=-2)
    own_blocks = lax.dynamic_slice_in_dim(aperture, (my_line * rows + my_row) * cols, cols, axis=0)
    slot_table = lax.dynamic_index_in_dim(
        own_blocks.reshape(cols, sides, rows, cols, CAP), my_col, 3, False
    )

    table = dft_matrix(samples)
    own = spectrum(shot_traces, table)

    stacked = own.reshape(shots, sides, rows, cols, BP, 2, NF)
    stacked = jnp.transpose(stacked, (1, 0, 2, 3, 4, 5, 6))
    spread = lax.all_to_all(stacked, "gy", split_axis=2, concat_axis=2, tiled=True)
    spread = jnp.transpose(spread, (0, 2, 1, 3, 4, 5, 6))
    side_cols = [
        lax.ppermute(spread[2], "line", up),
        spread[1],
        lax.ppermute(spread[0], "line", down),
    ]

    lanes = jnp.transpose(own, (0, 2, 3, 1, 4))
    spec_rows = lanes.size // NF
    payload = jnp.concatenate([lanes.reshape(spec_rows, NF), src_weight.reshape(-1, NF)], axis=0)
    carried = [payload]
    offsets = [0]
    forward = payload
    backward = payload
    split = payload.shape[0] // 16 * 8
    for step in range(1, cols // 2 + 1):
        if 2 * step == cols:
            head = lax.ppermute(forward[:split], "gz", right)
            tail = lax.ppermute(backward[split:], "gz", left)
            carried.append(jnp.concatenate([head, tail], axis=0))
            offsets.append(step)
            break
        forward = lax.ppermute(forward, "gz", right)
        carried.append(forward)
        offsets.append(-step)
        backward = lax.ppermute(backward, "gz", left)
        carried.append(backward)
        offsets.append(step)
    sources = (my_col + jnp.asarray(offsets, dtype=jnp.int32)) % cols
    ring = jnp.stack(carried)
    gathered = ring[:, :spec_rows].reshape((len(carried),) + lanes.shape)
    weights = lax.dynamic_index_in_dim(
        ring[:, spec_rows:].reshape((len(carried),) + src_weight.shape), my_col, 3, False
    )
    slots = jnp.take(slot_table, sources, axis=0)
    hit = slots[..., None] == jnp.arange(blocks, dtype=jnp.int32)
    dense = jnp.sum(jnp.where(hit[..., None], weights[:, :, :, :, None, :], 0.0), axis=3)
    dense = jnp.transpose(dense, (1, 2, 0, 4, 3))

    def side_part(s, t0=0, t1=None):
        lo, hi = spans[s]
        cols_s = jnp.take(side_cols[s][t0:t1], sources, axis=2)
        return combine(cols_s, dense[s, t0:t1, :, :, lo:hi], gathered[:, :, :, :, lo:hi])

    cut = rows // 2
    shifted = []
    for t0, t1 in ((0, cut), (cut, rows)):
        shifted.append((
            t0, t1,
            lax.ppermute(side_part(0, t0, t1), "line", down),
            lax.ppermute(side_part(2, t0, t1), "line", up),
        ))
    total = side_part(1)
    for t0, t1, from_up, from_down in shifted:
        total = total.at[t0:t1, :, :, :, width:].add(from_up)
        total = total.at[t0:t1, :, :, :, : 2 * width].add(from_down)
    result = lax.psum_scatter(total, "gy", scatter_dimension=0, tiled=False)
    result = jnp.transpose(result, (0, 3, 1, 2, 4))
    return result.reshape(shots, recv, 2, NF)


def grid_shape(mesh):
    row = mesh.devices[0]
    try:
        ys = sorted({d.coords[1] for d in row})
        zs = sorted({d.coords[2] for d in row})
        if len(ys) * len(zs) == len(row):
            return len(ys), len(zs)
    except Exception:
        pass
    return 4, len(row) // 4


def solution(mesh):
    rows, cols = grid_shape(mesh)
    lines = mesh.devices.shape[0]
    fine = Mesh(np.asarray(mesh.devices).reshape(lines, rows, cols), ("line", "gy", "gz"))
    split = ("line", "gy", "gz")
    mapped = jax.shard_map(
        body,
        mesh=fine,
        in_specs=(P(split, None, None), P(), P(split, None, None, None), P()),
        out_specs=P(split, None, None, None),
        check_vma=False,
    )
    out_sharding = NamedSharding(mesh, P(("line", "grp"), None, None, None))
    return jax.jit(mapped, out_shardings=out_sharding)
```
